1024 devices in a mesh: ctx: 128 (over z, y_lo, core), tp: 8 (over y_hi, x).
Axes of the slice: x: 4, y: 4 (y_hi: 2, y_lo: 2; y = y_hi * 2 + y_lo), z: 32, core: 2. Of those that a mesh axis runs over, the one named last changes fastest.
Arguments:
- signal: bfloat16 [16384, 4096], P('ctx', 'tp'), may hold values from -6 to 6
- gate: bfloat16 [16384, 4096], P('ctx', 'tp'), may hold values from -6 to 6
- skip: float32 [4096], P('tp'), may hold values from -1 to 1
- filter_taps: bfloat16 [16384, 4096], P('ctx', 'tp'), may hold values from -0.046875 to 0.046875
- out_weight: bfloat16 [4096, 4096], P('tp'), may hold values from -0.125 to 0.125
Outputs:
- mixed_out: bfloat16 [16384, 4096], P('ctx', 'tp')
The draws below stay inside these ranges and needn't reach their ends.
All inputs are finite; a program needn't handle non-finite values.
Results may differ from the reference program's by a relative error of at most 0.023.
Values may be sent and summed in bfloat16 or wider, within the bound.
No kernel may reach another device: no remote copies, remote signals or barrier semaphores. Data moves between devices by JAX's collectives and lax.ppermute only.
A program may use at most 64 MiB of HBM per device.

```python
import math
import jax
import jax.numpy as jnp
from jax import lax

TOK_DEV = 128
CH = 4096
OW = 4096
TOKENS = 16384
N_CTX = 128
N_TP = 8


def raised(drawn, rng, source, target, shards_of, factor):
    owner, partner = [(jnp.arange(drawn.shape[dim]) // (drawn.shape[dim] // shards_of)).reshape([-1 if axis == dim else 1 for axis in range(drawn.ndim)]) for dim in (source, target)]
    chosen = jax.random.permutation(rng, shards_of)[partner]
    strong = (owner == chosen) | (owner == (partner + shards_of // 2) % shards_of)
    return jnp.where(strong, factor * drawn, drawn)


def level_of(key, extent, cuts, low, high):
    factor_of = 1.0
    for axis_at, blocks in cuts:
        heights = jax.random.uniform(jax.random.fold_in(jax.random.fold_in(key, 6), axis_at), (blocks,), jnp.float32, low / len(cuts), high / len(cuts))
        factor_of = factor_of * jnp.repeat(jnp.exp(heights), extent[axis_at] // blocks).reshape((-1,) + (1,) * (len(extent) - 1 - axis_at))
    return factor_of


def scatter_about(stream_key, extent, deviation, limit, cuts=(), held_as=jnp.bfloat16):
    gain = level_of(stream_key, extent, cuts, -0.22, 0.18) if cuts else 1.0
    values = jax.random.normal(stream_key, extent, jnp.float32) * deviation * gain
    return jnp.minimum(jnp.maximum(values, -limit), limit).astype(held_as)


def gaussian_with(rng, dims, scale, bound, shards, heavy, kind=jnp.bfloat16):
    entries = scale * jax.random.normal(rng, dims, jnp.float32)
    if shards:
        entries = entries * level_of(rng, dims, shards, -0.22, 0.18)
    return jnp.clip(raised(entries, jax.random.fold_in(rng, 3), *heavy), -bound, bound).astype(kind)


def setup_inputs(seed: int = 0) -> dict:
    streams_of = jax.random.split(jax.random.key(seed), 6)
    signal = scatter_about(streams_of[0], (TOKENS, CH), 1.0, 6.0, ((0, 128), (1, 8)))
    gate = scatter_about(streams_of[1], (TOKENS, CH), 1.0, 6.0, ((0, 128), (1, 8)))
    skip = jnp.clip(jax.random.uniform(streams_of[2], (CH,), jnp.float32, -1.0, 1.0) * level_of(streams_of[2], (CH,), ((0, 8),), -0.4, 0.0), -1.0, 1.0)
    filter_taps = scatter_about(streams_of[3], (TOKENS, CH), TOKENS ** -0.5, 0.046875, ((0, 128), (1, 8)))
    out_weight = gaussian_with(streams_of[4], (CH, OW), CH ** -0.5, 0.125, ((0, 8),), (0, 1, 8, 2.0))
    return dict(signal=signal, gate=gate, skip=skip, filter_taps=filter_taps, out_weight=out_weight)


def rounded(values):
    narrow = lax.optimization_barrier(values.astype(jnp.bfloat16))
    return narrow.astype(jnp.float32)


def pair_up(real_part, imag_part, shape):
    return jnp.stack([real_part, imag_part], axis=1).reshape(shape)


def rotate(stack, cosine, sine):
    real_part = stack[0::2]
    imag_part = stack[1::2]
    return pair_up(real_part * cosine - imag_part * sine, real_part * sine + imag_part * cosine, stack.shape)


def multiply(stack, other):
    sr, si = stack[0::2], stack[1::2]
    hr, hi = other[0::2], other[1::2]
    return pair_up(sr * hr - si * hi, sr * hi + si * hr, stack.shape)


def panel_work(pieces):
    source, taps, gating, coeff = pieces
    length = source.shape[0]
    block = source.shape[1]
    levels = N_CTX.bit_length() - 1
    x = source.astype(jnp.float32)
    h = taps.astype(jnp.float32)
    angle = jnp.arange(length, dtype=jnp.int32).astype(jnp.float32) * (-math.pi / length)
    wr = jnp.cos(angle)[:, None]
    wi = jnp.sin(angle)[:, None]
    state = jnp.stack([x, jnp.zeros_like(x), x * wr, x * wi, h, jnp.zeros_like(h), h * wr, h * wi])
    for bit in reversed(range(levels)):
        span = TOK_DEV << bit
        view = rounded(state).reshape(8, length // (2 * span), 2, span, block)
        first = view[:, :, 0]
        second = view[:, :, 1]
        turn = jnp.arange(span, dtype=jnp.int32).astype(jnp.float32) * (-math.pi / span)
        low = first + second
        high = rotate(first - second, jnp.cos(turn)[:, None], jnp.sin(turn)[:, None])
        state = jnp.stack([low, high], axis=2).reshape(8, length, block)
    blocks = state.reshape(8, N_CTX, TOK_DEV, block)
    comp = blocks[0::2] + 1j * blocks[1::2]
    spec = jnp.fft.fft(comp, axis=2)
    state = pair_up(jnp.real(spec), jnp.imag(spec), (8, length, block)).astype(x.dtype)
    state = multiply(state[:4], state[4:])
    blocks = state.reshape(4, N_CTX, TOK_DEV, block)
    comp = blocks[0::2] + 1j * blocks[1::2]
    back = jnp.fft.ifft(comp, axis=2) * TOK_DEV
    state = pair_up(jnp.real(back), jnp.imag(back), (4, length, block)).astype(x.dtype)
    for bit in range(levels):
        span = TOK_DEV << bit
        view = rounded(state).reshape(4, length // (2 * span), 2, span, block)
        first = view[:, :, 0]
        turn = jnp.arange(span, dtype=jnp.int32).astype(jnp.float32) * (math.pi / span)
        other = rotate(view[:, :, 1], jnp.cos(turn)[:, None], jnp.sin(turn)[:, None])
        state = jnp.stack([first + other, first - other], axis=2).reshape(4, length, block)
    conv = (state[0] + wr * state[2] + wi * state[3]) / (2.0 * length)
    mixed = gating.astype(jnp.float32) * (conv + coeff[None, :] * x)
    return mixed.astype(jnp.bfloat16)


def reference(signal, gate, skip, filter_taps, out_weight):
    length = signal.shape[0]
    block = math.gcd(CH, 128)
    groups = CH // block
    source = signal.reshape(length, groups, block).transpose(1, 0, 2)
    taps = filter_taps.reshape(length, groups, block).transpose(1, 0, 2)
    gating = gate.reshape(length, groups, block).transpose(1, 0, 2)
    coeff = skip.reshape(groups, block)
    mixed = lax.map(panel_work, (source, taps, gating, coeff))
    mixed = mixed.transpose(1, 0, 2).reshape(length, CH)
    width = CH // N_TP
    total = jnp.zeros((length, OW), jnp.float32)
    for group in range(N_TP):
        partial_value = jnp.dot(mixed[:, group * width:(group + 1) * width], out_weight[group * width:(group + 1) * width], preferred_element_type=jnp.float32)
        total = total + rounded(partial_value)
    return total.astype(jnp.bfloat16)
```

```python
import math

import jax
import jax.numpy as jnp
import numpy as np
from jax import lax
from jax.sharding import PartitionSpec as P

LANES = 128


def dft_table(rows, cols, size, sign):
    grid = np.arange(rows)[:, None] * np.arange(cols)[None, :] % size
    angle = grid * (sign * 2.0 * math.pi / size)
    return np.cos(angle), np.sin(angle)


def as_bf16(values):
    return jnp.asarray(values, jnp.float32).astype(jnp.bfloat16)


def mm(spec, table, data):
    return jnp.einsum(spec, table, data.astype(jnp.bfloat16), preferred_element_type=jnp.float32)


def long_conv(x, h, length):
    per = x.shape[0]
    half = length // LANES
    full = 2 * half
    total = 2 * length
    f1r, f1i = (as_bf16(t) for t in dft_table(full, half, full, -1.0))
    f3r, f3i = (as_bf16(t) for t in dft_table(LANES, LANES, LANES, -1.0))
    twr, twi = (jnp.asarray(t, jnp.float32) for t in dft_table(full, LANES, total, -1.0))
    both = jnp.concatenate([x.reshape(per, half, LANES), h.reshape(per, half, LANES)])
    ar = mm("kp,spq->skq", f1r, both)
    ai = mm("kp,spq->skq", f1i, both)
    br = ar * twr - ai * twi
    bi = ar * twi + ai * twr
    xr = mm("skq,qm->skm", br, f3r) - mm("skq,qm->skm", bi, f3i)
    xi = mm("skq,qm->skm", br, f3i) + mm("skq,qm->skm", bi, f3r)
    zr = xr[:per] * xr[per:] - xi[:per] * xi[per:]
    zi = xr[:per] * xi[per:] + xi[:per] * xr[per:]
    ur = mm("skq,qm->skm", zr, f3r) + mm("skq,qm->skm", zi, f3i)
    ui = mm("skq,qm->skm", zi, f3r) - mm("skq,qm->skm", zr, f3i)
    vr = ur * twr + ui * twi
    vi = ui * twr - ur * twi
    conv = mm("kp,skq->spq", f1r, vr) + mm("kp,skq->spq", f1i, vi)
    return conv.reshape(per, length) * (1.0 / total)


def per_device(signal, gate, skip, filter_taps, out_weight):
    rows, width = signal.shape
    count = lax.axis_size("ctx")
    length = rows * count
    per = width // count
    stack = jnp.stack([signal, filter_taps, gate]).transpose(0, 2, 1)
    gathered = lax.all_to_all(stack, "ctx", 1, 2, tiled=True)
    conv = long_conv(gathered[0], gathered[1], length)
    source = gathered[0].astype(jnp.float32)
    coeff = lax.dynamic_slice(skip, (lax.axis_index("ctx") * per,), (per,))
    mixed = (gathered[2].astype(jnp.float32) * (conv + coeff[:, None] * source)).astype(jnp.bfloat16)
    back = lax.all_to_all(mixed, "ctx", 1, 0, tiled=True)
    partial_value = jnp.einsum("cr,co->ro", back, out_weight, preferred_element_type=jnp.float32)
    return lax.psum_scatter(
        partial_value.astype(jnp.bfloat16), "tp", scatter_dimension=1, tiled=True
    )


def solution(mesh):
    return jax.shard_map(
        per_device,
        mesh=mesh,
        in_specs=(P("ctx", "tp"), P("ctx", "tp"), P("tp"), P("ctx", "tp"), P("tp", None)),
        out_specs=P("ctx", "tp"),
        check_vma=False,
    )
```

```python
import math

import jax
import jax.numpy as jnp
import numpy as np
from jax import lax
from jax.sharding import PartitionSpec as P

LANES = 128


def dft_table(rows, cols, size, sign):
    grid = np.arange(rows)[:, None] * np.arange(cols)[None, :] % size
    angle = grid * (sign * 2.0 * math.pi / size)
    return np.cos(angle), np.sin(angle)


def as_bf16(values):
    return jnp.asarray(values, jnp.float32).astype(jnp.bfloat16)


def mm(spec, table, data):
    return jnp.einsum(spec, table, data.astype(jnp.bfloat16), preferred_element_type=jnp.float32)


def long_conv(x, h, length):
    per = x.shape[0]
    half = length // LANES
    full = 2 * half
    total = 2 * length
    f1r, f1i = (as_bf16(t) for t in dft_table(full, half, full, -1.0))
    f3r, f3i = (as_bf16(t) for t in dft_table(LANES, LANES, LANES, -1.0))
    twr, twi = (jnp.asarray(t, jnp.float32) for t in dft_table(full, LANES, total, -1.0))
    both = jnp.concatenate([x.reshape(per, half, LANES), h.reshape(per, half, LANES)])
    ar = mm("kp,spq->skq", f1r, both)
    ai = mm("kp,spq->skq", f1i, both)
    br = ar * twr - ai * twi
    bi = ar * twi + ai * twr
    xr = mm("skq,qm->skm", br, f3r) - mm("skq,qm->skm", bi, f3i)
    xi = mm("skq,qm->skm", br, f3i) + mm("skq,qm->skm", bi, f3r)
    zr = xr[:per] * xr[per:] - xi[:per] * xi[per:]
    zi = xr[:per] * xi[per:] + xi[:per] * xr[per:]
    ur = mm("skq,qm->skm", zr, f3r) + mm("skq,qm->skm", zi, f3i)
    ui = mm("skq,qm->skm", zi, f3r) - mm("skq,qm->skm", zr, f3i)
    vr = ur * twr + ui * twi
    vi = ui * twr - ur * twi
    conv = mm("kp,skq->spq", f1r, vr) + mm("kp,skq->spq", f1i, vi)
    return conv.reshape(per, length) * (1.0 / total)


def per_device(signal, gate, skip, filter_taps, out_weight):
    rows, width = signal.shape
    count = lax.axis_size("ctx")
    length = rows * count
    per = width // count
    stack = jnp.stack([signal, filter_taps, gate]).transpose(0, 2, 1)
    gathered = lax.all_to_all(stack, "ctx", 1, 2, tiled=True)
    conv = long_conv(gathered[0], gathered[1], length)
    source = gathered[0].astype(jnp.float32)
    coeff = lax.dynamic_slice(skip, (lax.axis_index("ctx") * per,), (per,))
    mixed = (gathered[2].astype(jnp.float32) * (conv + coeff[:, None] * source)).astype(jnp.bfloat16)
    back = lax.all_to_all(mixed, "ctx", 1, 0, tiled=True)
    partial_value = jnp.einsum("cr,co->ro", back, out_weight, preferred_element_type=jnp.float32)
    return halving_scatter(partial_value.astype(jnp.bfloat16), "tp")


def halving_scatter(value, axis):
    count = lax.axis_size(axis)
    index = lax.axis_index(axis)
    rows, cols = value.shape
    levels = count.bit_length() - 1
    blocks = value.reshape(rows, *([2] * levels), cols // count)
    total = None
    for bit in range(levels):
        dim = levels - bit
        upper = (index >> bit & 1) == 1
        low = lax.index_in_dim(blocks, 0, dim, keepdims=False)
        high = lax.index_in_dim(blocks, 1, dim, keepdims=False)
        keep = jnp.where(upper, high, low)
        sent = jnp.where(upper, low, high)
        got = lax.ppermute(sent, axis, [(i, i ^ 1 << bit) for i in range(count)])
        total = keep.astype(jnp.float32) + got.astype(jnp.float32)
        blocks = total.astype(jnp.bfloat16)
    return total.reshape(rows, cols // count).astype(jnp.bfloat16)


def solution(mesh):
    return jax.shard_map(
        per_device,
        mesh=mesh,
        in_specs=(P("ctx", "tp"), P("ctx", "tp"), P("tp"), P("ctx", "tp"), P("tp", None)),
        out_specs=P("ctx", "tp"),
        check_vma=False,
    )
```

```python
import math

import jax
import jax.numpy as jnp
import numpy as np
from jax import lax
from jax.sharding import PartitionSpec as P

LANES = 128


def dft_table(rows, cols, size, sign):
    grid = np.arange(rows)[:, None] * np.arange(cols)[None, :] % size
    angle = grid * (sign * 2.0 * math.pi / size)
    return np.cos(angle), np.sin(angle)


def as_bf16(values):
    return jnp.asarray(values, jnp.float32).astype(jnp.bfloat16)


def mm(spec, table, data):
    return jnp.einsum(spec, table, data.astype(jnp.bfloat16), preferred_element_type=jnp.float32)


def long_conv(x, h, length):
    per = x.shape[0]
    half = length // LANES
    full = 2 * half
    total = 2 * length
    f1r, f1i = (as_bf16(t) for t in dft_table(full, half, full, -1.0))
    f3r, f3i = (as_bf16(t) for t in dft_table(LANES, LANES, LANES, -1.0))
    twr, twi = (jnp.asarray(t, jnp.float32) for t in dft_table(full, LANES, total, -1.0))
    both = jnp.concatenate([x.reshape(per, half, LANES), h.reshape(per, half, LANES)])
    ar = mm("kp,spq->skq", f1r, both)
    ai = mm("kp,spq->skq", f1i, both)
    br = ar * twr - ai * twi
    bi = ar * twi + ai * twr
    xr = mm("skq,qm->skm", br, f3r) - mm("skq,qm->skm", bi, f3i)
    xi = mm("skq,qm->skm", br, f3i) + mm("skq,qm->skm", bi, f3r)
    zr = xr[:per] * xr[per:] - xi[:per] * xi[per:]
    zi = xr[:per] * xi[per:] + xi[:per] * xr[per:]
    ur = mm("skq,qm->skm", zr, f3r) + mm("skq,qm->skm", zi, f3i)
    ui = mm("skq,qm->skm", zi, f3r) - mm("skq,qm->skm", zr, f3i)
    vr = ur * twr + ui * twi
    vi = ui * twr - ur * twi
    conv = mm("kp,skq->spq", f1r, vr) + mm("kp,skq->spq", f1i, vi)
    return conv.reshape(per, length) * (1.0 / total)


def per_device(signal, gate, skip, filter_taps, out_weight):
    rows, width = signal.shape
    count = lax.axis_size("ctx")
    length = rows * count
    stack = jnp.stack([signal, filter_taps]).transpose(0, 2, 1)
    gathered = lax.all_to_all(stack, "ctx", 1, 2, tiled=True)
    conv = long_conv(gathered[0], gathered[1], length).astype(jnp.bfloat16)
    back = lax.all_to_all(conv, "ctx", 1, 0, tiled=True).astype(jnp.float32).T
    source = signal.astype(jnp.float32)
    mixed = (gate.astype(jnp.float32) * (back + skip[None, :] * source)).astype(jnp.bfloat16)
    partial_value = jnp.dot(mixed, out_weight, preferred_element_type=jnp.float32)
    return halving_scatter(partial_value.astype(jnp.bfloat16), "tp")


def halving_scatter(value, axis):
    count = lax.axis_size(axis)
    index = lax.axis_index(axis)
    rows, cols = value.shape
    levels = count.bit_length() - 1
    blocks = value.reshape(rows, *([2] * levels), cols // count)
    total = None
    for bit in range(levels):
        dim = levels - bit
        upper = (index >> bit & 1) == 1
        low = lax.index_in_dim(blocks, 0, dim, keepdims=False)
        high = lax.index_in_dim(blocks, 1, dim, keepdims=False)
        keep = jnp.where(upper, high, low)
        sent = jnp.where(upper, low, high)
        got = lax.ppermute(sent, axis, [(i, i ^ 1 << bit) for i in range(count)])
        total = keep.astype(jnp.float32) + got.astype(jnp.float32)
        blocks = total.astype(jnp.bfloat16)
    return total.reshape(rows, cols // count).astype(jnp.bfloat16)


def solution(mesh):
    return jax.shard_map(
        per_device,
        mesh=mesh,
        in_specs=(P("ctx", "tp"), P("ctx", "tp"), P("tp"), P("ctx", "tp"), P("tp", None)),
        out_specs=P("ctx", "tp"),
        check_vma=False,
    )
```

```python
import math

import jax
import jax.numpy as jnp
import numpy as np
from jax import lax
from jax.sharding import PartitionSpec as P

LANES = 128


def dft_table(rows, cols, size, sign):
    grid = np.arange(rows)[:, None] * np.arange(cols)[None, :] % size
    angle = grid * (sign * 2.0 * math.pi / size)
    return np.cos(angle), np.sin(angle)


def as_bf16(values):
    return jnp.asarray(values, jnp.float32).astype(jnp.bfloat16)


def mm(spec, table, data):
    return jnp.einsum(spec, table, data.astype(jnp.bfloat16), preferred_element_type=jnp.float32)


def long_conv(x, h, length):
    per = x.shape[0]
    half = length // LANES
    full = 2 * half
    total = 2 * length
    f1r, f1i = (as_bf16(t) for t in dft_table(full, half, full, -1.0))
    f3r, f3i = (as_bf16(t) for t in dft_table(LANES, LANES, LANES, -1.0))
    twr, twi = (jnp.asarray(t, jnp.float32) for t in dft_table(full, LANES, total, -1.0))
    both = jnp.concatenate([x.reshape(per, half, LANES), h.reshape(per, half, LANES)])
    ar = mm("kp,spq->skq", f1r, both)
    ai = mm("kp,spq->skq", f1i, both)
    br = ar * twr - ai * twi
    bi = ar * twi + ai * twr
    xr = mm("skq,qm->skm", br, f3r) - mm("skq,qm->skm", bi, f3i)
    xi = mm("skq,qm->skm", br, f3i) + mm("skq,qm->skm", bi, f3r)
    zr = xr[:per] * xr[per:] - xi[:per] * xi[per:]
    zi = xr[:per] * xi[per:] + xi[:per] * xr[per:]
    ur = mm("skq,qm->skm", zr, f3r) + mm("skq,qm->skm", zi, f3i)
    ui = mm("skq,qm->skm", zi, f3r) - mm("skq,qm->skm", zr, f3i)
    vr = ur * twr + ui * twi
    vi = ui * twr - ur * twi
    conv = mm("kp,skq->spq", f1r, vr) + mm("kp,skq->spq", f1i, vi)
    return conv.reshape(per, length) * (1.0 / total)


def per_device(signal, gate, skip, filter_taps, out_weight):
    rows, width = signal.shape
    count = lax.axis_size("ctx")
    length = rows * count
    stack = jnp.stack([signal, filter_taps]).transpose(0, 2, 1)
    gathered = lax.all_to_all(stack, "ctx", 1, 2, tiled=True)
    conv = long_conv(gathered[0], gathered[1], length).astype(jnp.bfloat16)
    back = lax.all_to_all(conv, "ctx", 1, 0, tiled=True).astype(jnp.float32).T
    source = signal.astype(jnp.float32)
    mixed = (gate.astype(jnp.float32) * (back + skip[None, :] * source)).astype(jnp.bfloat16)
    partial_value = jnp.dot(mixed, out_weight, preferred_element_type=jnp.float32)
    return exchange_scatter(partial_value.astype(jnp.bfloat16), "tp")


def exchange_scatter(value, axis):
    count = lax.axis_size(axis)
    rows, cols = value.shape
    parts = lax.all_to_all(value.reshape(rows, count, cols // count), axis, 1, 1, tiled=True)
    return parts.astype(jnp.float32).sum(1).astype(jnp.bfloat16)


def solution(mesh):
    return jax.shard_map(
        per_device,
        mesh=mesh,
        in_specs=(P("ctx", "tp"), P("ctx", "tp"), P("tp"), P("ctx", "tp"), P("tp", None)),
        out_specs=P("ctx", "tp"),
        check_vma=False,
    )
```

```python
import math

import jax
import jax.numpy as jnp
import numpy as np
from jax import lax
from jax.sharding import PartitionSpec as P

LANES = 128


def dft_table(rows, cols, size, sign):
    grid = np.arange(rows)[:, None] * np.arange(cols)[None, :] % size
    angle = grid * (sign * 2.0 * math.pi / size)
    return np.cos(angle), np.sin(angle)


def as_bf16(values):
    return jnp.asarray(values, jnp.float32).astype(jnp.bfloat16)


def mm(spec, table, data):
    return jnp.einsum(spec, table, data.astype(jnp.bfloat16), preferred_element_type=jnp.float32)


def long_conv(x, h, length):
    per = x.shape[0]
    half = length // LANES
    full = 2 * half
    total = 2 * length
    f1r, f1i = dft_table(full, half, full, -1.0)
    f3r, f3i = dft_table(LANES, LANES, LANES, -1.0)
    first = as_bf16(np.concatenate([f1r, f1i]))
    third = as_bf16(np.block([[f3r, f3i], [-f3i, f3r]]))
    twr, twi = (jnp.asarray(t, jnp.float32) for t in dft_table(full, LANES, total, -1.0))
    both = jnp.concatenate([x.reshape(per, half, LANES), h.reshape(per, half, LANES)])
    a = mm("kp,spq->skq", first, both)
    ar, ai = a[:, :full], a[:, full:]
    b = jnp.concatenate([ar * twr - ai * twi, ar * twi + ai * twr], axis=2)
    spec = mm("skq,qm->skm", b, third)
    xr, xi = spec[:per, :, :LANES], spec[:per, :, LANES:]
    hr, hi = spec[per:, :, :LANES], spec[per:, :, LANES:]
    z = jnp.concatenate([xr * hr - xi * hi, xr * hi + xi * hr], axis=2)
    u = mm("skm,qm->skq", z, third)
    ur, ui = u[:, :, :LANES], u[:, :, LANES:]
    v = jnp.concatenate([ur * twr + ui * twi, ui * twr - ur * twi], axis=1)
    conv = mm("kp,skq->spq", first, v)
    return conv.reshape(per, length) * (1.0 / total)


def per_device(signal, gate, skip, filter_taps, out_weight):
    rows, width = signal.shape
    count = lax.axis_size("ctx")
    length = rows * count
    stack = jnp.stack([signal, filter_taps]).transpose(0, 2, 1)
    gathered = lax.all_to_all(stack, "ctx", 1, 2, tiled=True)
    conv = long_conv(gathered[0], gathered[1], length).astype(jnp.bfloat16)
    back = lax.all_to_all(conv, "ctx", 1, 0, tiled=True).astype(jnp.float32).T
    source = signal.astype(jnp.float32)
    mixed = (gate.astype(jnp.float32) * (back + skip[None, :] * source)).astype(jnp.bfloat16)
    partial_value = jnp.dot(mixed, out_weight, preferred_element_type=jnp.float32)
    return exchange_scatter(partial_value.astype(jnp.bfloat16), "tp")


def exchange_scatter(value, axis):
    count = lax.axis_size(axis)
    rows, cols = value.shape
    parts = lax.all_to_all(value.reshape(rows, count, cols // count), axis, 1, 1, tiled=True)
    return parts.astype(jnp.float32).sum(1).astype(jnp.bfloat16)


def solution(mesh):
    return jax.shard_map(
        per_device,
        mesh=mesh,
        in_specs=(P("ctx", "tp"), P("ctx", "tp"), P("tp"), P("ctx", "tp"), P("tp", None)),
        out_specs=P("ctx", "tp"),
        check_vma=False,
    )
```

```python
import math

import jax
import jax.numpy as jnp
import numpy as np
from jax import lax
from jax.sharding import PartitionSpec as P

LANES = 128


def dft_table(rows, cols, size, sign):
    grid = np.arange(rows)[:, None] * np.arange(cols)[None, :] % size
    angle = grid * (sign * 2.0 * math.pi / size)
    return np.cos(angle), np.sin(angle)


def as_bf16(values):
    return jnp.asarray(values, jnp.float32).astype(jnp.bfloat16)


def mm(spec, table, data):
    return jnp.einsum(spec, table, data.astype(jnp.bfloat16), preferred_element_type=jnp.float32)


def long_conv(x, h, length):
    per = x.shape[0]
    half = length // LANES
    full = 2 * half
    total = 2 * length
    f1r, f1i = dft_table(full, half, full, -1.0)
    f3r, f3i = dft_table(LANES, LANES, LANES, -1.0)
    first = as_bf16(np.concatenate([f1r, f1i]))
    third = as_bf16(np.block([[f3r, f3i], [-f3i, f3r]]))
    twr, twi = (jnp.asarray(t, jnp.float32) for t in dft_table(full, LANES, total, -1.0))
    both = jnp.concatenate([x.reshape(per, half, LANES), h.reshape(per, half, LANES)])
    a = mm("kp,spq->skq", first, both)
    ar, ai = a[:, :full], a[:, full:]
    b = jnp.concatenate([ar * twr - ai * twi, ar * twi + ai * twr], axis=2)
    spec = mm("skq,qm->skm", b, third)
    xr, xi = spec[:per, :, :LANES], spec[:per, :, LANES:]
    hr, hi = spec[per:, :, :LANES], spec[per:, :, LANES:]
    z = jnp.concatenate([xr * hr - xi * hi, xr * hi + xi * hr], axis=2)
    u = mm("skm,qm->skq", z, third)
    ur, ui = u[:, :, :LANES], u[:, :, LANES:]
    v = jnp.concatenate([ur * twr + ui * twi, ui * twr - ur * twi], axis=1)
    conv = mm("kp,skq->spq", first, v)
    return conv.reshape(per, length) * (1.0 / total)


def per_device(signal, gate, skip, filter_taps, out_weight):
    rows, width = signal.shape
    count = lax.axis_size("ctx")
    length = rows * count
    stack = jnp.stack([signal, filter_taps]).transpose(0, 2, 1)
    gathered = lax.all_to_all(stack, "ctx", 1, 2, tiled=True)
    conv = long_conv(gathered[0], gathered[1], length).astype(jnp.bfloat16)
    back = lax.all_to_all(conv, "ctx", 1, 0, tiled=True).astype(jnp.float32)
    source = signal.T.astype(jnp.float32)
    mixed = (gate.T.astype(jnp.float32) * (back + skip[:, None] * source)).astype(jnp.bfloat16)
    partial_value = jnp.einsum("co,ct->ot", out_weight, mixed, preferred_element_type=jnp.float32)
    return exchange_scatter(partial_value.astype(jnp.bfloat16), "tp").T


def exchange_scatter(value, axis):
    count = lax.axis_size(axis)
    rows, cols = value.shape
    parts = lax.all_to_all(value.reshape(count, rows // count, cols), axis, 0, 0, tiled=True)
    return parts.astype(jnp.float32).sum(0).astype(jnp.bfloat16)


def solution(mesh):
    return jax.shard_map(
        per_device,
        mesh=mesh,
        in_specs=(P("ctx", "tp"), P("ctx", "tp"), P("tp"), P("ctx", "tp"), P("tp", None)),
        out_specs=P("ctx", "tp"),
        check_vma=False,
    )
```

```python
import math

import jax
import jax.numpy as jnp
import numpy as np
from jax import lax
from jax.sharding import PartitionSpec as P

LANES = 128


def dft_table(rows, cols, size, sign):
    grid = np.arange(rows)[:, None] * np.arange(cols)[None, :] % size
    angle = grid * (sign * 2.0 * math.pi / size)
    return np.cos(angle), np.sin(angle)


def as_bf16(values):
    return jnp.asarray(values, jnp.float32).astype(jnp.bfloat16)


def mm(spec, table, data):
    return jnp.einsum(spec, table, data.astype(jnp.bfloat16), preferred_element_type=jnp.float32)


def long_conv(x, h, length):
    per = x.shape[0]
    half = length // LANES
    full = 2 * half
    total = 2 * length
    f1r, f1i = dft_table(full, half, full, -1.0)
    f3r, f3i = dft_table(LANES, LANES, LANES, -1.0)
    first = as_bf16(np.concatenate([f1r, f1i]))
    third = as_bf16(np.block([[f3r, f3i], [-f3i, f3r]]))
    twr, twi = (jnp.asarray(t, jnp.float32) for t in dft_table(full, LANES, total, -1.0))
    both = jnp.concatenate([x.reshape(per, half, LANES), h.reshape(per, half, LANES)])
    a = mm("kp,spq->skq", first, both)
    ar, ai = a[:, :full], a[:, full:]
    b = jnp.concatenate([ar * twr - ai * twi, ar * twi + ai * twr], axis=2)
    spec = mm("skq,qm->skm", b, third)
    xr, xi = spec[:per, :, :LANES], spec[:per, :, LANES:]
    hr, hi = spec[per:, :, :LANES], spec[per:, :, LANES:]
    z = jnp.concatenate([xr * hr - xi * hi, xr * hi + xi * hr], axis=2)
    u = mm("skm,qm->skq", z, third)
    ur, ui = u[:, :, :LANES], u[:, :, LANES:]
    v = jnp.concatenate([ur * twr + ui * twi, ui * twr - ur * twi], axis=1)
    last = as_bf16(np.concatenate([f1r, f1i]) / total)
    return mm("kp,skq->psq", last, v)


def per_device(signal, gate, skip, filter_taps, out_weight):
    rows, width = signal.shape
    count = lax.axis_size("ctx")
    length = rows * count
    stack = jnp.stack([signal, filter_taps]).transpose(0, 2, 1)
    gathered = lax.all_to_all(stack, "ctx", 1, 2, tiled=True)
    conv = long_conv(gathered[0], gathered[1], length).astype(jnp.bfloat16)
    back = lax.all_to_all(conv, "ctx", 0, 0, tiled=True).reshape(width, rows).astype(jnp.float32)
    source = signal.T.astype(jnp.float32)
    mixed = (gate.T.astype(jnp.float32) * (back + skip[:, None] * source)).astype(jnp.bfloat16)
    partial_value = jnp.einsum("co,ct->ot", out_weight, mixed, preferred_element_type=jnp.float32)
    return exchange_scatter(partial_value.astype(jnp.bfloat16), "tp").T


def exchange_scatter(value, axis):
    count = lax.axis_size(axis)
    rows, cols = value.shape
    parts = lax.all_to_all(value.reshape(count, rows // count, cols), axis, 0, 0, tiled=True)
    return parts.astype(jnp.float32).sum(0).astype(jnp.bfloat16)


def solution(mesh):
    return jax.shard_map(
        per_device,
        mesh=mesh,
        in_specs=(P("ctx", "tp"), P("ctx", "tp"), P("tp"), P("ctx", "tp"), P("tp", None)),
        out_specs=P("ctx", "tp"),
        check_vma=False,
    )
```

```python
import math

import jax
import jax.numpy as jnp
import numpy as np
from jax import lax
from jax.sharding import PartitionSpec as P

LANES = 128


def dft_table(rows, cols, size, sign):
    grid = np.arange(rows)[:, None] * np.arange(cols)[None, :] % size
    angle = grid * (sign * 2.0 * math.pi / size)
    return np.cos(angle), np.sin(angle)


def as_bf16(values):
    return jnp.asarray(values, jnp.float32).astype(jnp.bfloat16)


def mm(spec, table, data):
    return jnp.einsum(spec, table, data.astype(jnp.bfloat16), preferred_element_type=jnp.float32)


def long_conv(x, h, length):
    per = x.shape[0]
    half = length // LANES
    full = 2 * half
    total = 2 * length
    f1r, f1i = dft_table(full, half, full, -1.0)
    f3r, f3i = dft_table(LANES, LANES, LANES, -1.0)
    first = as_bf16(np.concatenate([f1r, f1i]))
    third = as_bf16(np.block([[f3r, f3i], [-f3i, f3r]]))
    twr, twi = (jnp.asarray(t, jnp.float32) for t in dft_table(full, LANES, total, -1.0))
    both = jnp.concatenate([x.reshape(per, half, LANES), h.reshape(per, half, LANES)])
    a = mm("kp,spq->skq", first, both)
    ar, ai = a[:, :full], a[:, full:]
    b = jnp.concatenate([ar * twr - ai * twi, ar * twi + ai * twr], axis=2)
    spec = mm("skq,qm->skm", b, third)
    xr, xi = spec[:per, :, :LANES], spec[:per, :, LANES:]
    hr, hi = spec[per:, :, :LANES], spec[per:, :, LANES:]
    z = jnp.concatenate([xr * hr - xi * hi, xr * hi + xi * hr], axis=2)
    u = mm("skm,qm->skq", z, third)
    ur, ui = u[:, :, :LANES], u[:, :, LANES:]
    v = jnp.concatenate([ur * twr + ui * twi, ui * twr - ur * twi], axis=1)
    conv = mm("kp,skq->spq", first, v)
    return conv.reshape(per, length) * (1.0 / total)


def per_device(signal, gate, skip, filter_taps, out_weight):
    rows, width = signal.shape
    count = lax.axis_size("ctx")
    length = rows * count
    stack = jnp.stack([signal, filter_taps]).transpose(0, 2, 1)
    gathered = lax.all_to_all(stack, "ctx", 1, 2, tiled=True)
    conv = long_conv(gathered[0], gathered[1], length).astype(jnp.bfloat16)
    back = lax.all_to_all(conv, "ctx", 1, 0, tiled=True).astype(jnp.float32)
    gating = gate.T.astype(jnp.float32)
    skipped = (gating * skip[:, None] * signal.T.astype(jnp.float32)).astype(jnp.bfloat16)
    early = jnp.einsum("co,ct->ot", out_weight, skipped, preferred_element_type=jnp.float32)
    gated = (gating * back).astype(jnp.bfloat16)
    partial_value = early + jnp.einsum("co,ct->ot", out_weight, gated, preferred_element_type=jnp.float32)
    return exchange_scatter(partial_value.astype(jnp.bfloat16), "tp").T


def exchange_scatter(value, axis):
    count = lax.axis_size(axis)
    rows, cols = value.shape
    parts = lax.all_to_all(value.reshape(count, rows // count, cols), axis, 0, 0, tiled=True)
    return parts.astype(jnp.float32).sum(0).astype(jnp.bfloat16)


def solution(mesh):
    return jax.shard_map(
        per_device,
        mesh=mesh,
        in_specs=(P("ctx", "tp"), P("ctx", "tp"), P("tp"), P("ctx", "tp"), P("tp", None)),
        out_specs=P("ctx", "tp"),
        check_vma=False,
    )
```
